256 devices in a mesh: gx: 16 (over z_lo, x, core), gy: 16 (over z_hi, y).
Axes of the slice: x: 4, y: 4, z: 8 (z_hi: 4, z_lo: 2; z = z_hi * 2 + z_lo), core: 2. Of those that a mesh axis runs over, the one named last changes fastest.
Arguments:
- species_field: float32 [4, 1024, 256, 256], P(None, 'gx', 'gy'), may hold values from -400 to 400
- initial: float32 [1024, 128], replicated, may hold values from -6 to 6
Outputs:
- factor: float32 [1024, 128], replicated
- gram_two: float32 [256, 256], replicated
The draws below stay inside these ranges and needn't reach their ends.
All inputs are finite; a program needn't handle non-finite values.
Results may differ from the reference program's by a relative error of at most 0.0002.
Values sent between devices are 32-bit elements; how exact they have to be, the bound alone decides.
No kernel may reach another device: no remote copies, remote signals or barrier semaphores. Data moves between devices by JAX's collectives and lax.ppermute only.
A program may use at most 128 MiB of HBM per device.

```python
import math
import jax
import jax.numpy as jnp
from jax import lax

S = 4
NX = 1024
NY = 256
NZ = 256
R = 128
SWEEPS = 3


def draw_species_field(key, part):
    subkeys = jax.random.split(key, 5)
    shape = (S, NX, NY, NZ)
    values_base = jax.random.truncated_normal(subkeys[0], -6.0, 6.0, shape, jnp.float32)
    scale_x = jnp.exp(jax.random.uniform(subkeys[1], (NX,), jnp.float32, math.log(0.3), math.log(3.0)))
    ramp_y = 1.0 + 2.0 * jnp.arange(NY, dtype=jnp.float32) / NY
    scale_y = jnp.exp(jax.random.uniform(subkeys[2], (NY,), jnp.float32, math.log(0.5), math.log(2.0))) * ramp_y
    ramp_z = 1.0 + 2.0 * jnp.arange(NZ, dtype=jnp.float32) / NZ
    scale_z = jnp.exp(jax.random.uniform(subkeys[3], (NZ,), jnp.float32, math.log(0.5), math.log(2.0))) * ramp_z
    scale_s = jnp.exp(jax.random.uniform(subkeys[4], (S,), jnp.float32, math.log(0.5), math.log(2.0)))
    scaled = values_base * scale_x[None, :, None, None] * scale_y[None, None, :, None]
    scaled = scaled * scale_z[None, None, None, :] * scale_s[:, None, None, None]
    return scaled * 0.25


def scatter_about(stream_key, extent, width, reach, kind=jnp.bfloat16):
    array = width * jax.random.normal(stream_key, extent, jnp.float32)
    return jnp.clip(array, min=-reach, max=reach).astype(kind)


def setup_inputs(seed: int = 0) -> dict:
    seeds = jax.random.split(jax.random.key(seed), 3)
    species_field = draw_species_field(jax.random.fold_in(seeds[2], 71), 0)
    initial = scatter_about(seeds[1], (NX, R), 1.0, 6.0, jnp.float32)
    return {"species_field": species_field, "initial": initial}


def reference(species_field, initial):
    highest = lax.Precision.HIGHEST
    gram_one = jnp.zeros((NX, NX), jnp.float32)
    for spec_index in range(S):
        matrix = species_field[spec_index].reshape(NX, NY * NZ)
        gram_one = gram_one + jnp.dot(matrix.astype(jnp.float32), matrix.T.astype(jnp.float32), precision=highest, preferred_element_type=jnp.float32)
    gram_one = gram_one / (S * NY * NZ)
    basis = initial
    for sweep_index in range(SWEEPS):
        wide = jnp.dot(gram_one.astype(jnp.float32), basis.astype(jnp.float32), precision=highest, preferred_element_type=jnp.float32)
        square = jnp.dot(wide.T.astype(jnp.float32), wide.astype(jnp.float32), precision=highest, preferred_element_type=jnp.float32)
        factor_low = jnp.linalg.cholesky(square)
        basis = jax.scipy.linalg.solve_triangular(factor_low, wide.T, lower=True).T
    gram_two = jnp.zeros((NY, NY), jnp.float32)
    for spec_index in range(S):
        matrix = species_field[spec_index].reshape(NX, NY * NZ)
        core_tensor = jnp.dot(basis.T.astype(jnp.float32), matrix.astype(jnp.float32), precision=highest, preferred_element_type=jnp.float32).reshape(R, NY, NZ)
        gram_two = gram_two + jnp.einsum('ryz,rwz->yw', core_tensor, core_tensor, precision=highest)
    gram_two = gram_two / (S * R * NZ)
    return (basis * math.sqrt(NX), gram_two)
```

```python
import math

import jax
import jax.numpy as jnp
from jax import lax
from jax.sharding import PartitionSpec as P

S = 4
NY = 256
NZ = 256
R = 128
SWEEPS = 3


def butterfly_sum(value, axis, size):
    stride = 1
    while stride < size:
        value = value + lax.ppermute(value, axis, [(i, i ^ stride) for i in range(size)])
        stride *= 2
    return value


def body(species_field, initial):
    highest = lax.Precision.HIGHEST
    regrouped = lax.all_to_all(species_field, "gx", split_axis=3, concat_axis=1, tiled=True)
    species, rows_x, cols_y, slab_z = regrouped.shape
    fibers = regrouped.reshape(species, rows_x, cols_y * slab_z)
    scale_one = 1.0 / (S * NY * NZ)
    basis = initial
    gram_one = lax.psum(
        jnp.einsum("sxc,swc->xw", fibers, fibers, precision=highest) * scale_one, ("gx", "gy")
    )
    for sweep_index in range(SWEEPS):
        wide = jnp.dot(gram_one, basis, precision=highest, preferred_element_type=jnp.float32)
        square = jnp.dot(wide.T, wide, precision=highest, preferred_element_type=jnp.float32)
        factor_low = jnp.linalg.cholesky(square)
        basis = jax.scipy.linalg.solve_triangular(factor_low, wide.T, lower=True).T
    core_tensor = jnp.einsum("xr,sxc->src", basis, fibers, precision=highest)
    core_blocks = core_tensor.reshape(species, R, cols_y, slab_z)
    blocks = lax.all_to_all(core_blocks, "gy", split_axis=1, concat_axis=2, tiled=True)
    second_part = jnp.einsum("sryz,srwz->yw", blocks, blocks, precision=highest) / (S * R * NZ)
    gram_two = butterfly_sum(second_part, "gx", lax.axis_size("gx"))
    gram_two = butterfly_sum(gram_two, "gy", lax.axis_size("gy"))
    return (basis * math.sqrt(rows_x), gram_two)


def solution(mesh):
    placed = (P(None, "gx", "gy", None), P())
    return jax.shard_map(body, mesh=mesh, in_specs=placed, out_specs=(P(), P()), check_vma=False)
```

```python
import math

import jax
import jax.numpy as jnp
from jax import lax
from jax.sharding import PartitionSpec as P

S = 4
NY = 256
NZ = 256
R = 128
SWEEPS = 3
BLOCK = 128


def butterfly_sum(value, axis, size):
    stride = 1
    while stride < size:
        value = value + lax.ppermute(value, axis, [(i, i ^ stride) for i in range(size)])
        stride *= 2
    return value


def halving_steps(sizes):
    steps = []
    for axis, size in sizes:
        stride = size // 2
        while stride >= 1:
            steps.append((axis, size, stride))
            stride //= 2
    return steps


def halving_doubling_sum(value, sizes):
    steps = halving_steps(sizes)
    for axis, size, stride in steps:
        upper = (lax.axis_index(axis) // stride) % 2 == 1
        half = value.shape[0] // 2
        low, high = value[:half], value[half:]
        keep = jnp.where(upper, high, low)
        send = jnp.where(upper, low, high)
        value = keep + lax.ppermute(send, axis, [(i, i ^ stride) for i in range(size)])
    for axis, size, stride in reversed(steps):
        upper = (lax.axis_index(axis) // stride) % 2 == 1
        other = lax.ppermute(value, axis, [(i, i ^ stride) for i in range(size)])
        value = jnp.where(upper, jnp.concatenate([other, value]), jnp.concatenate([value, other]))
    return value


def body(species_field, initial):
    highest = lax.Precision.HIGHEST
    regrouped = lax.all_to_all(species_field, "gx", split_axis=3, concat_axis=1, tiled=True)
    species, rows_x, cols_y, slab_z = regrouped.shape
    fibers = regrouped.reshape(species, rows_x, cols_y * slab_z)
    scale_one = 1.0 / (S * NY * NZ)
    n_blocks = rows_x // BLOCK
    lower = []
    for row in range(n_blocks):
        strip = jnp.einsum(
            "sxc,swc->xw",
            fibers[:, row * BLOCK:(row + 1) * BLOCK],
            fibers[:, :(row + 1) * BLOCK],
            precision=highest,
        ) * scale_one
        lower.extend(strip[:, col * BLOCK:(col + 1) * BLOCK] for col in range(row + 1))
    packed = jnp.concatenate(lower, axis=0)
    sizes = (("gx", lax.axis_size("gx")), ("gy", lax.axis_size("gy")))
    packed = halving_doubling_sum(packed, sizes)
    blocks = packed.reshape(-1, BLOCK, BLOCK)
    index = {}
    for row in range(n_blocks):
        for col in range(row + 1):
            index[(row, col)] = len(index)
    gram_one = jnp.concatenate([
        jnp.concatenate([
            blocks[index[(row, col)]] if col <= row else blocks[index[(col, row)]].T
            for col in range(n_blocks)
        ], axis=1)
        for row in range(n_blocks)
    ], axis=0)
    basis = initial
    for sweep_index in range(SWEEPS):
        wide = jnp.dot(gram_one, basis, precision=highest, preferred_element_type=jnp.float32)
        square = jnp.dot(wide.T, wide, precision=highest, preferred_element_type=jnp.float32)
        factor_low = jnp.linalg.cholesky(square)
        basis = jax.scipy.linalg.solve_triangular(factor_low, wide.T, lower=True).T
    core_tensor = jnp.einsum("xr,sxc->src", basis, fibers, precision=highest)
    core_blocks = core_tensor.reshape(species, R, cols_y, slab_z)
    blocks = lax.all_to_all(core_blocks, "gy", split_axis=1, concat_axis=2, tiled=True)
    second_part = jnp.einsum("sryz,srwz->yw", blocks, blocks, precision=highest) / (S * R * NZ)
    gram_two = butterfly_sum(second_part, "gx", lax.axis_size("gx"))
    gram_two = butterfly_sum(gram_two, "gy", lax.axis_size("gy"))
    return (basis * math.sqrt(rows_x), gram_two)


def solution(mesh):
    placed = (P(None, "gx", "gy", None), P())
    return jax.shard_map(body, mesh=mesh, in_specs=placed, out_specs=(P(), P()), check_vma=False)
```

```python
import math

import jax
import jax.numpy as jnp
from jax import lax
from jax.sharding import PartitionSpec as P

S = 4
NY = 256
NZ = 256
R = 128
SWEEPS = 3
BLOCK = 128


def butterfly_sum(value, axis, size):
    stride = 1
    while stride < size:
        value = value + lax.ppermute(value, axis, [(i, i ^ stride) for i in range(size)])
        stride *= 2
    return value


def halving_steps(sizes):
    steps = []
    for axis, size in sizes:
        stride = size // 2
        while stride >= 1:
            steps.append((axis, size, stride))
            stride //= 2
    return steps


def halving_doubling_sum(value, sizes):
    steps = halving_steps(sizes)
    for axis, size, stride in steps:
        upper = (lax.axis_index(axis) // stride) % 2 == 1
        half = value.shape[0] // 2
        low, high = value[:half], value[half:]
        keep = jnp.where(upper, high, low)
        send = jnp.where(upper, low, high)
        value = keep + lax.ppermute(send, axis, [(i, i ^ stride) for i in range(size)])
    for axis, size, stride in reversed(steps):
        upper = (lax.axis_index(axis) // stride) % 2 == 1
        other = lax.ppermute(value, axis, [(i, i ^ stride) for i in range(size)])
        value = jnp.where(upper, jnp.concatenate([other, value]), jnp.concatenate([value, other]))
    return value


def body(species_field, initial):
    highest = lax.Precision.HIGHEST
    regrouped = lax.all_to_all(species_field, "gx", split_axis=3, concat_axis=1, tiled=True)
    species, rows_x, cols_y, slab_z = regrouped.shape
    fibers = regrouped.reshape(species, rows_x, cols_y * slab_z)
    scale_one = 1.0 / (S * NY * NZ)
    n_blocks = rows_x // BLOCK
    lower = []
    for row in range(n_blocks):
        strip = jnp.einsum(
            "sxc,swc->xw",
            fibers[:, row * BLOCK:(row + 1) * BLOCK],
            fibers[:, :(row + 1) * BLOCK],
            precision=highest,
        ) * scale_one
        lower.extend(strip[:, col * BLOCK:(col + 1) * BLOCK] for col in range(row + 1))
    packed = jnp.concatenate(lower, axis=0)
    sizes = (("gx", lax.axis_size("gx")), ("gy", lax.axis_size("gy")))
    packed = halving_doubling_sum(packed, sizes)
    blocks = packed.reshape(-1, BLOCK, BLOCK)
    both = jnp.concatenate([blocks, jnp.swapaxes(blocks, 1, 2)], axis=0)
    index = {}
    for row in range(n_blocks):
        for col in range(row + 1):
            index[(row, col)] = len(index)
    picks = [[index[(row, col)] if col <= row else len(index) + index[(col, row)]
              for col in range(n_blocks)] for row in range(n_blocks)]
    tiles = jnp.take(both, jnp.asarray(picks, jnp.int32), axis=0)
    gram_one = jnp.swapaxes(tiles, 1, 2).reshape(rows_x, rows_x)
    basis = initial
    for sweep_index in range(SWEEPS):
        wide = jnp.dot(gram_one, basis, precision=highest, preferred_element_type=jnp.float32)
        square = jnp.dot(wide.T, wide, precision=highest, preferred_element_type=jnp.float32)
        factor_low = jnp.linalg.cholesky(square)
        basis = jax.scipy.linalg.solve_triangular(factor_low, wide.T, lower=True).T
    core_tensor = jnp.einsum("xr,sxc->src", basis, fibers, precision=highest)
    core_blocks = core_tensor.reshape(species, R, cols_y, slab_z)
    blocks = lax.all_to_all(core_blocks, "gy", split_axis=1, concat_axis=2, tiled=True)
    second_part = jnp.einsum("sryz,srwz->yw", blocks, blocks, precision=highest) / (S * R * NZ)
    gram_two = butterfly_sum(second_part, "gx", lax.axis_size("gx"))
    gram_two = butterfly_sum(gram_two, "gy", lax.axis_size("gy"))
    return (basis * math.sqrt(rows_x), gram_two)


def solution(mesh):
    placed = (P(None, "gx", "gy", None), P())
    return jax.shard_map(body, mesh=mesh, in_specs=placed, out_specs=(P(), P()), check_vma=False)
```

```python
import math

import jax
import jax.numpy as jnp
from jax import lax
from jax.sharding import PartitionSpec as P

S = 4
NY = 256
NZ = 256
R = 128
SWEEPS = 3
BLOCK = 128


def butterfly_sum(value, axis, size):
    stride = 1
    while stride < size:
        value = value + lax.ppermute(value, axis, [(i, i ^ stride) for i in range(size)])
        stride *= 2
    return value


def halving_steps(sizes):
    steps = []
    for axis, size in sizes:
        stride = size // 2
        while stride >= 1:
            steps.append((axis, size, stride))
            stride //= 2
    return steps


def halving_doubling_sum(value, sizes):
    steps = halving_steps(sizes)
    for axis, size, stride in steps:
        upper = (lax.axis_index(axis) // stride) % 2 == 1
        half = value.shape[0] // 2
        low, high = value[:half], value[half:]
        keep = jnp.where(upper, high, low)
        send = jnp.where(upper, low, high)
        value = keep + lax.ppermute(send, axis, [(i, i ^ stride) for i in range(size)])
    for axis, size, stride in reversed(steps):
        upper = (lax.axis_index(axis) // stride) % 2 == 1
        other = lax.ppermute(value, axis, [(i, i ^ stride) for i in range(size)])
        value = jnp.where(upper, jnp.concatenate([other, value]), jnp.concatenate([value, other]))
    return value


def body(species_field, initial):
    highest = lax.Precision.HIGHEST
    regrouped = lax.all_to_all(species_field, "gx", split_axis=3, concat_axis=1, tiled=True)
    species, rows_x, cols_y, slab_z = regrouped.shape
    fibers = regrouped.reshape(species, rows_x, cols_y * slab_z)
    scale_one = 1.0 / (S * NY * NZ)
    n_blocks = rows_x // BLOCK
    lower = []
    for row in range(n_blocks):
        strip = jnp.einsum(
            "sxc,swc->xw",
            fibers[:, row * BLOCK:(row + 1) * BLOCK],
            fibers[:, :(row + 1) * BLOCK],
            precision=highest,
        ) * scale_one
        lower.extend(strip[:, col * BLOCK:(col + 1) * BLOCK] for col in range(row + 1))
    packed = jnp.concatenate(lower, axis=0)
    sizes = (("gx", lax.axis_size("gx")), ("gy", lax.axis_size("gy")))
    packed = halving_doubling_sum(packed, sizes)
    blocks = packed.reshape(-1, BLOCK, BLOCK)
    both = jnp.concatenate([blocks, jnp.swapaxes(blocks, 1, 2)], axis=0)
    index = {}
    for row in range(n_blocks):
        for col in range(row + 1):
            index[(row, col)] = len(index)
    picks = [[index[(row, col)] if col <= row else len(index) + index[(col, row)]
              for col in range(n_blocks)] for row in range(n_blocks)]
    tiles = jnp.take(both, jnp.asarray(picks, jnp.int32), axis=0)
    gram_one = jnp.swapaxes(tiles, 1, 2).reshape(rows_x, rows_x)
    def sweep(sweep_index, basis):
        wide = jnp.dot(gram_one, basis, precision=highest, preferred_element_type=jnp.float32)
        square = jnp.dot(wide.T, wide, precision=highest, preferred_element_type=jnp.float32)
        factor_low = jnp.linalg.cholesky(square)
        return jax.scipy.linalg.solve_triangular(factor_low, wide.T, lower=True).T

    basis = lax.fori_loop(0, SWEEPS, sweep, initial)
    core_tensor = jnp.einsum("xr,sxc->src", basis, fibers, precision=highest)
    core_blocks = core_tensor.reshape(species, R, cols_y, slab_z)
    blocks = lax.all_to_all(core_blocks, "gy", split_axis=1, concat_axis=2, tiled=True)
    second_part = jnp.einsum("sryz,srwz->yw", blocks, blocks, precision=highest) / (S * R * NZ)
    gram_two = butterfly_sum(second_part, "gx", lax.axis_size("gx"))
    gram_two = butterfly_sum(gram_two, "gy", lax.axis_size("gy"))
    return (basis * math.sqrt(rows_x), gram_two)


def solution(mesh):
    placed = (P(None, "gx", "gy", None), P())
    return jax.shard_map(body, mesh=mesh, in_specs=placed, out_specs=(P(), P()), check_vma=False)
```

```python
import math

import jax
import jax.numpy as jnp
from jax import lax
from jax.sharding import PartitionSpec as P

S = 4
NY = 256
NZ = 256
R = 128
SWEEPS = 3
BLOCK = 128


def butterfly_sum(value, axis, size):
    stride = 1
    while stride < size:
        value = value + lax.ppermute(value, axis, [(i, i ^ stride) for i in range(size)])
        stride *= 2
    return value


def halving_steps(sizes):
    steps = []
    for axis, size in sizes:
        stride = size // 2
        while stride >= 1:
            steps.append((axis, size, stride))
            stride //= 2
    return steps


def halving_doubling_sum(value, sizes):
    steps = halving_steps(sizes)
    for axis, size, stride in steps:
        upper = (lax.axis_index(axis) // stride) % 2 == 1
        half = value.shape[0] // 2
        low, high = value[:half], value[half:]
        keep = jnp.where(upper, high, low)
        send = jnp.where(upper, low, high)
        value = keep + lax.ppermute(send, axis, [(i, i ^ stride) for i in range(size)])
    for axis, size, stride in reversed(steps):
        upper = (lax.axis_index(axis) // stride) % 2 == 1
        other = lax.ppermute(value, axis, [(i, i ^ stride) for i in range(size)])
        value = jnp.where(upper, jnp.concatenate([other, value]), jnp.concatenate([value, other]))
    return value


def body(species_field, initial):
    highest = lax.Precision.HIGHEST
    by_row = jnp.moveaxis(species_field, 2, 0)
    regrouped = lax.all_to_all(by_row, "gx", split_axis=0, concat_axis=0, tiled=True)
    x_blocks, species, block_x, slab_z = regrouped.shape
    rows_x = x_blocks * block_x
    fibers = jnp.swapaxes(regrouped, 0, 1).reshape(species, rows_x, slab_z)
    scale_one = 1.0 / (S * NY * NZ)
    n_blocks = rows_x // BLOCK
    lower = []
    for row in range(n_blocks):
        strip = jnp.einsum(
            "sxc,swc->xw",
            fibers[:, row * BLOCK:(row + 1) * BLOCK],
            fibers[:, :(row + 1) * BLOCK],
            precision=highest,
        ) * scale_one
        lower.extend(strip[:, col * BLOCK:(col + 1) * BLOCK] for col in range(row + 1))
    packed = jnp.concatenate(lower, axis=0)
    sizes = (("gx", lax.axis_size("gx")), ("gy", lax.axis_size("gy")))
    packed = halving_doubling_sum(packed, sizes)
    blocks = packed.reshape(-1, BLOCK, BLOCK)
    both = jnp.concatenate([blocks, jnp.swapaxes(blocks, 1, 2)], axis=0)
    index = {}
    for row in range(n_blocks):
        for col in range(row + 1):
            index[(row, col)] = len(index)
    picks = [[index[(row, col)] if col <= row else len(index) + index[(col, row)]
              for col in range(n_blocks)] for row in range(n_blocks)]
    tiles = jnp.take(both, jnp.asarray(picks, jnp.int32), axis=0)
    gram_one = jnp.swapaxes(tiles, 1, 2).reshape(rows_x, rows_x)
    basis = initial
    for sweep_index in range(SWEEPS):
        wide = jnp.dot(gram_one, basis, precision=highest, preferred_element_type=jnp.float32)
        square = jnp.dot(wide.T, wide, precision=highest, preferred_element_type=jnp.float32)
        factor_low = jnp.linalg.cholesky(square)
        basis = jax.scipy.linalg.solve_triangular(factor_low, wide.T, lower=True).T
    core_tensor = jnp.einsum("xr,sxc->src", basis, fibers, precision=highest)
    n_gy = lax.axis_size("gy")
    n_gx = lax.axis_size("gx")
    by_rank = jnp.swapaxes(core_tensor.reshape(species, n_gy, R // n_gy, slab_z), 0, 1)
    stage_one = lax.all_to_all(by_rank, "gy", split_axis=0, concat_axis=0, tiled=True)
    pairs = stage_one.reshape(n_gy, n_gx, species * (R // n_gy) // n_gx, slab_z)
    stage_two = lax.all_to_all(jnp.swapaxes(pairs, 0, 1), "gx", split_axis=0, concat_axis=0, tiled=True)
    columns = jnp.swapaxes(stage_two, 0, 1).reshape(n_gy * n_gx, -1)
    second_part = jnp.einsum("yc,wc->yw", columns, columns, precision=highest) / (S * R * NZ)
    gram_two = butterfly_sum(second_part, "gx", lax.axis_size("gx"))
    gram_two = butterfly_sum(gram_two, "gy", lax.axis_size("gy"))
    return (basis * math.sqrt(rows_x), gram_two)


def solution(mesh):
    placed = (P(None, "gx", "gy", None), P())
    return jax.shard_map(body, mesh=mesh, in_specs=placed, out_specs=(P(), P()), check_vma=False)
```

```python
import math

import jax
import jax.numpy as jnp
from jax import lax
from jax.sharding import PartitionSpec as P

S = 4
NY = 256
NZ = 256
R = 128
SWEEPS = 3
BLOCK = 128


def butterfly_sum(value, axis, size):
    stride = 1
    while stride < size:
        value = value + lax.ppermute(value, axis, [(i, i ^ stride) for i in range(size)])
        stride *= 2
    return value


def halving_steps(sizes):
    steps = []
    for axis, size in sizes:
        stride = size // 2
        while stride >= 1:
            steps.append((axis, size, stride))
            stride //= 2
    return steps


def halving_step(value, axis, size, stride):
    upper = (lax.axis_index(axis) // stride) % 2 == 1
    half = value.shape[0] // 2
    low, high = value[:half], value[half:]
    keep = jnp.where(upper, high, low)
    send = jnp.where(upper, low, high)
    return keep + lax.ppermute(send, axis, [(i, i ^ stride) for i in range(size)])


def doubling_step(value, axis, size, stride):
    upper = (lax.axis_index(axis) // stride) % 2 == 1
    other = lax.ppermute(value, axis, [(i, i ^ stride) for i in range(size)])
    return jnp.where(upper, jnp.concatenate([other, value]), jnp.concatenate([value, other]))


def halving_doubling_sum(value, sizes):
    half = value.shape[0] // 2
    chains = [value[:half], value[half:]]
    orders = [halving_steps(sizes), halving_steps(tuple(reversed(sizes)))]
    for index in range(len(orders[0])):
        chains = [halving_step(chain, *order[index]) for chain, order in zip(chains, orders)]
    for index in reversed(range(len(orders[0]))):
        chains = [doubling_step(chain, *order[index]) for chain, order in zip(chains, orders)]
    return jnp.concatenate(chains)


def body(species_field, initial):
    highest = lax.Precision.HIGHEST
    by_row = jnp.moveaxis(species_field, 2, 0)
    regrouped = lax.all_to_all(by_row, "gx", split_axis=0, concat_axis=0, tiled=True)
    x_blocks, species, block_x, slab_z = regrouped.shape
    rows_x = x_blocks * block_x
    fibers = jnp.swapaxes(regrouped, 0, 1).reshape(species, rows_x, slab_z)
    scale_one = 1.0 / (S * NY * NZ)
    n_blocks = rows_x // BLOCK
    lower = []
    for row in range(n_blocks):
        strip = jnp.einsum(
            "sxc,swc->xw",
            fibers[:, row * BLOCK:(row + 1) * BLOCK],
            fibers[:, :(row + 1) * BLOCK],
            precision=highest,
        ) * scale_one
        lower.extend(strip[:, col * BLOCK:(col + 1) * BLOCK] for col in range(row + 1))
    packed = jnp.concatenate(lower, axis=0)
    sizes = (("gx", lax.axis_size("gx")), ("gy", lax.axis_size("gy")))
    packed = halving_doubling_sum(packed, sizes)
    blocks = packed.reshape(-1, BLOCK, BLOCK)
    both = jnp.concatenate([blocks, jnp.swapaxes(blocks, 1, 2)], axis=0)
    index = {}
    for row in range(n_blocks):
        for col in range(row + 1):
            index[(row, col)] = len(index)
    picks = [[index[(row, col)] if col <= row else len(index) + index[(col, row)]
              for col in range(n_blocks)] for row in range(n_blocks)]
    tiles = jnp.take(both, jnp.asarray(picks, jnp.int32), axis=0)
    gram_one = jnp.swapaxes(tiles, 1, 2).reshape(rows_x, rows_x)
    basis = initial
    for sweep_index in range(SWEEPS):
        wide = jnp.dot(gram_one, basis, precision=highest, preferred_element_type=jnp.float32)
        square = jnp.dot(wide.T, wide, precision=highest, preferred_element_type=jnp.float32)
        factor_low = jnp.linalg.cholesky(square)
        basis = jax.scipy.linalg.solve_triangular(factor_low, wide.T, lower=True).T
    core_tensor = jnp.einsum("xr,sxc->src", basis, fibers, precision=highest)
    n_gy = lax.axis_size("gy")
    n_gx = lax.axis_size("gx")
    by_rank = jnp.swapaxes(core_tensor.reshape(species, n_gy, R // n_gy, slab_z), 0, 1)
    stage_one = lax.all_to_all(by_rank, "gy", split_axis=0, concat_axis=0, tiled=True)
    pairs = stage_one.reshape(n_gy, n_gx, species * (R // n_gy) // n_gx, slab_z)
    stage_two = lax.all_to_all(jnp.swapaxes(pairs, 0, 1), "gx", split_axis=0, concat_axis=0, tiled=True)
    columns = jnp.swapaxes(stage_two, 0, 1).reshape(n_gy * n_gx, -1)
    second_part = jnp.einsum("yc,wc->yw", columns, columns, precision=highest) / (S * R * NZ)
    gram_two = halving_doubling_sum(second_part.reshape(-1, BLOCK), sizes).reshape(second_part.shape)
    return (basis * math.sqrt(rows_x), gram_two)


def solution(mesh):
    placed = (P(None, "gx", "gy", None), P())
    return jax.shard_map(body, mesh=mesh, in_specs=placed, out_specs=(P(), P()), check_vma=False)
```

```python
import math

import jax
import jax.numpy as jnp
from jax import lax
from jax.sharding import PartitionSpec as P

S = 4
NY = 256
NZ = 256
R = 128
SWEEPS = 3
BLOCK = 128


def butterfly_sum(value, axis, size):
    stride = 1
    while stride < size:
        value = value + lax.ppermute(value, axis, [(i, i ^ stride) for i in range(size)])
        stride *= 2
    return value


def halving_steps(sizes):
    steps = []
    for axis, size in sizes:
        stride = size // 2
        while stride >= 1:
            steps.append((axis, size, stride))
            stride //= 2
    return steps


def halving_doubling_sum(value, sizes):
    steps = halving_steps(sizes)
    for axis, size, stride in steps:
        upper = (lax.axis_index(axis) // stride) % 2 == 1
        half = value.shape[0] // 2
        low, high = value[:half], value[half:]
        keep = jnp.where(upper, high, low)
        send = jnp.where(upper, low, high)
        value = keep + lax.ppermute(send, axis, [(i, i ^ stride) for i in range(size)])
    for axis, size, stride in reversed(steps):
        upper = (lax.axis_index(axis) // stride) % 2 == 1
        other = lax.ppermute(value, axis, [(i, i ^ stride) for i in range(size)])
        value = jnp.where(upper, jnp.concatenate([other, value]), jnp.concatenate([value, other]))
    return value


def body(species_field, initial):
    highest = lax.Precision.HIGHEST
    by_row = jnp.moveaxis(species_field, 2, 0)
    regrouped = lax.all_to_all(by_row, "gx", split_axis=0, concat_axis=0, tiled=True)
    x_blocks, species, block_x, slab_z = regrouped.shape
    rows_x = x_blocks * block_x
    fibers = jnp.swapaxes(regrouped, 0, 1).reshape(species, rows_x, slab_z)
    scale_one = 1.0 / (S * NY * NZ)
    n_blocks = rows_x // BLOCK
    lower = []
    for row in range(n_blocks):
        strip = jnp.einsum(
            "sxc,swc->xw",
            fibers[:, row * BLOCK:(row + 1) * BLOCK],
            fibers[:, :(row + 1) * BLOCK],
            precision=highest,
        ) * scale_one
        lower.extend(strip[:, col * BLOCK:(col + 1) * BLOCK] for col in range(row + 1))
    packed = jnp.concatenate(lower, axis=0)
    sizes = (("gx", lax.axis_size("gx")), ("gy", lax.axis_size("gy")))
    packed = halving_doubling_sum(packed, sizes)
    blocks = packed.reshape(-1, BLOCK, BLOCK)
    both = jnp.concatenate([blocks, jnp.swapaxes(blocks, 1, 2)], axis=0)
    index = {}
    for row in range(n_blocks):
        for col in range(row + 1):
            index[(row, col)] = len(index)
    picks = [[index[(row, col)] if col <= row else len(index) + index[(col, row)]
              for col in range(n_blocks)] for row in range(n_blocks)]
    tiles = jnp.take(both, jnp.asarray(picks, jnp.int32), axis=0)
    gram_one = jnp.swapaxes(tiles, 1, 2).reshape(rows_x, rows_x)
    basis = initial
    for sweep_index in range(SWEEPS):
        wide = jnp.dot(gram_one, basis, precision=highest, preferred_element_type=jnp.float32)
        square = jnp.dot(wide.T, wide, precision=highest, preferred_element_type=jnp.float32)
        factor_low = jnp.linalg.cholesky(square)
        basis = lax.linalg.triangular_solve(factor_low, wide, left_side=False, lower=True, transpose_a=True)
    core_tensor = jnp.einsum("xr,sxc->src", basis, fibers, precision=highest)
    n_gy = lax.axis_size("gy")
    n_gx = lax.axis_size("gx")
    by_rank = jnp.swapaxes(core_tensor.reshape(species, n_gy, R // n_gy, slab_z), 0, 1)
    stage_one = lax.all_to_all(by_rank, "gy", split_axis=0, concat_axis=0, tiled=True)
    pairs = stage_one.reshape(n_gy, n_gx, species * (R // n_gy) // n_gx, slab_z)
    stage_two = lax.all_to_all(jnp.swapaxes(pairs, 0, 1), "gx", split_axis=0, concat_axis=0, tiled=True)
    columns = jnp.swapaxes(stage_two, 0, 1).reshape(n_gy * n_gx, -1)
    second_part = jnp.einsum("yc,wc->yw", columns, columns, precision=highest) / (S * R * NZ)
    half_y = second_part.shape[0] // 2
    lower_two = jnp.stack([second_part[:half_y, :half_y], second_part[half_y:, :half_y], second_part[half_y:, half_y:]])
    lower_two = butterfly_sum(lower_two, "gx", lax.axis_size("gx"))
    lower_two = butterfly_sum(lower_two, "gy", lax.axis_size("gy"))
    gram_two = jnp.concatenate([
        jnp.concatenate([lower_two[0], lower_two[1].T], axis=1),
        jnp.concatenate([lower_two[1], lower_two[2]], axis=1),
    ], axis=0)
    return (basis * math.sqrt(rows_x), gram_two)


def solution(mesh):
    placed = (P(None, "gx", "gy", None), P())
    return jax.shard_map(body, mesh=mesh, in_specs=placed, out_specs=(P(), P()), check_vma=False)
```

```python
import math

import jax
import jax.numpy as jnp
from jax import lax
from jax.sharding import PartitionSpec as P

S = 4
NY = 256
NZ = 256
R = 128
SWEEPS = 3
BLOCK = 128


def butterfly_sum(value, axis, size):
    stride = 1
    while stride < size:
        value = value + lax.ppermute(value, axis, [(i, i ^ stride) for i in range(size)])
        stride *= 2
    return value


def halving_steps(sizes):
    steps = []
    for axis, size in sizes:
        stride = size // 2
        while stride >= 1:
            steps.append((axis, size, stride))
            stride //= 2
    return steps


def halving_doubling_sum(value, sizes):
    steps = halving_steps(sizes)
    for axis, size, stride in steps:
        upper = (lax.axis_index(axis) // stride) % 2 == 1
        half = value.shape[0] // 2
        low, high = value[:half], value[half:]
        keep = jnp.where(upper, high, low)
        send = jnp.where(upper, low, high)
        value = keep + lax.ppermute(send, axis, [(i, i ^ stride) for i in range(size)])
    for axis, size, stride in reversed(steps):
        upper = (lax.axis_index(axis) // stride) % 2 == 1
        other = lax.ppermute(value, axis, [(i, i ^ stride) for i in range(size)])
        value = jnp.where(upper, jnp.concatenate([other, value]), jnp.concatenate([value, other]))
    return value


def body(species_field, initial):
    highest = lax.Precision.HIGHEST
    by_row = jnp.moveaxis(species_field, 2, 0)
    regrouped = lax.all_to_all(by_row, "gx", split_axis=0, concat_axis=0, tiled=True)
    x_blocks, species, block_x, slab_z = regrouped.shape
    rows_x = x_blocks * block_x
    fibers = jnp.swapaxes(regrouped, 0, 1).reshape(species, rows_x, slab_z)
    scale_one = 1.0 / (S * NY * NZ)
    n_blocks = rows_x // BLOCK
    lower = []
    for row in range(n_blocks):
        strip = jnp.einsum(
            "sxc,swc->xw",
            fibers[:, row * BLOCK:(row + 1) * BLOCK],
            fibers[:, :(row + 1) * BLOCK],
            precision=highest,
        ) * scale_one
        lower.extend(strip[:, col * BLOCK:(col + 1) * BLOCK] for col in range(row + 1))
    packed = jnp.concatenate(lower, axis=0)
    sizes = (("gx", lax.axis_size("gx")), ("gy", lax.axis_size("gy")))
    packed = halving_doubling_sum(packed, sizes)
    blocks = packed.reshape(-1, BLOCK, BLOCK)
    both = jnp.concatenate([blocks, jnp.swapaxes(blocks, 1, 2)], axis=0)
    index = {}
    for row in range(n_blocks):
        for col in range(row + 1):
            index[(row, col)] = len(index)
    picks = [[index[(row, col)] if col <= row else len(index) + index[(col, row)]
              for col in range(n_blocks)] for row in range(n_blocks)]
    tiles = jnp.take(both, jnp.asarray(picks, jnp.int32), axis=0)
    gram_one = jnp.swapaxes(tiles, 1, 2).reshape(rows_x, rows_x)
    basis = initial
    for sweep_index in range(SWEEPS):
        wide = jnp.dot(gram_one, basis, precision=highest, preferred_element_type=jnp.float32)
        square = jnp.dot(wide.T, wide, precision=highest, preferred_element_type=jnp.float32)
        factor_low = jnp.linalg.cholesky(square)
        basis = lax.linalg.triangular_solve(factor_low, wide, left_side=False, lower=True, transpose_a=True)
    core_tensor = jnp.einsum("xr,sxc->src", basis, fibers, precision=highest)
    n_gy = lax.axis_size("gy")
    n_gx = lax.axis_size("gx")
    pairs = core_tensor.reshape(n_gx * n_gy, -1, slab_z)
    gathered = lax.all_to_all(pairs, ("gx", "gy"), split_axis=0, concat_axis=0, tiled=True)
    columns = jnp.swapaxes(gathered.reshape(n_gx, n_gy, -1), 0, 1).reshape(n_gy * n_gx, -1)
    second_part = jnp.einsum("yc,wc->yw", columns, columns, precision=highest) / (S * R * NZ)
    half_y = second_part.shape[0] // 2
    lower_two = jnp.stack([second_part[:half_y, :half_y], second_part[half_y:, :half_y], second_part[half_y:, half_y:]])
    lower_two = butterfly_sum(lower_two, "gx", lax.axis_size("gx"))
    lower_two = butterfly_sum(lower_two, "gy", lax.axis_size("gy"))
    gram_two = jnp.concatenate([
        jnp.concatenate([lower_two[0], lower_two[1].T], axis=1),
        jnp.concatenate([lower_two[1], lower_two[2]], axis=1),
    ], axis=0)
    return (basis * math.sqrt(rows_x), gram_two)


def solution(mesh):
    placed = (P(None, "gx", "gy", None), P())
    return jax.shard_map(body, mesh=mesh, in_specs=placed, out_specs=(P(), P()), check_vma=False)
```

```python
import math

import jax
import jax.numpy as jnp
from jax import lax
from jax.sharding import PartitionSpec as P

S = 4
NY = 256
NZ = 256
R = 128
SWEEPS = 3
BLOCK = 128


def butterfly_sum(value, axis, size):
    stride = 1
    while stride < size:
        value = value + lax.ppermute(value, axis, [(i, i ^ stride) for i in range(size)])
        stride *= 2
    return value


def halving_steps(sizes):
    steps = []
    for axis, size in sizes:
        stride = size // 2
        while stride >= 1:
            steps.append((axis, size, stride))
            stride //= 2
    return steps


def halving_doubling_sum(value, sizes, middle=None):
    steps = halving_steps(sizes)
    for axis, size, stride in steps:
        upper = (lax.axis_index(axis) // stride) % 2 == 1
        half = value.shape[0] // 2
        low, high = value[:half], value[half:]
        keep = jnp.where(upper, high, low)
        send = jnp.where(upper, low, high)
        value = keep + lax.ppermute(send, axis, [(i, i ^ stride) for i in range(size)])
    if middle is not None:
        value = middle(value)
    for axis, size, stride in reversed(steps):
        upper = (lax.axis_index(axis) // stride) % 2 == 1
        other = lax.ppermute(value, axis, [(i, i ^ stride) for i in range(size)])
        value = jnp.where(upper, jnp.concatenate([other, value]), jnp.concatenate([value, other]))
    return value


def body(species_field, initial):
    highest = lax.Precision.HIGHEST
    by_row = jnp.moveaxis(species_field, 2, 0)
    regrouped = lax.all_to_all(by_row, "gx", split_axis=0, concat_axis=0, tiled=True)
    x_blocks, species, block_x, slab_z = regrouped.shape
    rows_x = x_blocks * block_x
    fibers = jnp.swapaxes(regrouped, 0, 1).reshape(species, rows_x, slab_z)
    scale_one = 1.0 / (S * NY * NZ)
    n_blocks = rows_x // BLOCK
    lower = []
    for row in range(n_blocks):
        strip = jnp.einsum(
            "sxc,swc->xw",
            fibers[:, row * BLOCK:(row + 1) * BLOCK],
            fibers[:, :(row + 1) * BLOCK],
            precision=highest,
        ) * scale_one
        lower.extend(strip[:, col * BLOCK:(col + 1) * BLOCK] for col in range(row + 1))
    packed = jnp.concatenate(lower, axis=0)
    sizes = (("gx", lax.axis_size("gx")), ("gy", lax.axis_size("gy")))
    packed = halving_doubling_sum(packed, sizes[:1], middle=lambda chunk: butterfly_sum(chunk, *sizes[1]))
    blocks = packed.reshape(-1, BLOCK, BLOCK)
    both = jnp.concatenate([blocks, jnp.swapaxes(blocks, 1, 2)], axis=0)
    index = {}
    for row in range(n_blocks):
        for col in range(row + 1):
            index[(row, col)] = len(index)
    picks = [[index[(row, col)] if col <= row else len(index) + index[(col, row)]
              for col in range(n_blocks)] for row in range(n_blocks)]
    tiles = jnp.take(both, jnp.asarray(picks, jnp.int32), axis=0)
    gram_one = jnp.swapaxes(tiles, 1, 2).reshape(rows_x, rows_x)
    basis = initial
    for sweep_index in range(SWEEPS):
        wide = jnp.dot(gram_one, basis, precision=highest, preferred_element_type=jnp.float32)
        square = jnp.dot(wide.T, wide, precision=highest, preferred_element_type=jnp.float32)
        factor_low = jnp.linalg.cholesky(square)
        basis = lax.linalg.triangular_solve(factor_low, wide, left_side=False, lower=True, transpose_a=True)
    core_tensor = jnp.einsum("xr,sxc->src", basis, fibers, precision=highest)
    n_gy = lax.axis_size("gy")
    n_gx = lax.axis_size("gx")
    pairs = core_tensor.reshape(n_gx * n_gy, -1, slab_z)
    gathered = lax.all_to_all(pairs, ("gx", "gy"), split_axis=0, concat_axis=0, tiled=True)
    columns = jnp.swapaxes(gathered.reshape(n_gx, n_gy, -1), 0, 1).reshape(n_gy * n_gx, -1)
    second_part = jnp.einsum("yc,wc->yw", columns, columns, precision=highest) / (S * R * NZ)
    half_y = second_part.shape[0] // 2
    lower_two = jnp.stack([second_part[:half_y, :half_y], second_part[half_y:, :half_y], second_part[half_y:, half_y:]])
    lower_two = butterfly_sum(lower_two, "gx", lax.axis_size("gx"))
    lower_two = butterfly_sum(lower_two, "gy", lax.axis_size("gy"))
    gram_two = jnp.concatenate([
        jnp.concatenate([lower_two[0], lower_two[1].T], axis=1),
        jnp.concatenate([lower_two[1], lower_two[2]], axis=1),
    ], axis=0)
    return (basis * math.sqrt(rows_x), gram_two)


def solution(mesh):
    placed = (P(None, "gx", "gy", None), P())
    return jax.shard_map(body, mesh=mesh, in_specs=placed, out_specs=(P(), P()), check_vma=False)
```

```python
import math

import jax
import jax.numpy as jnp
from jax import lax
from jax.sharding import PartitionSpec as P

S = 4
NY = 256
NZ = 256
R = 128
SWEEPS = 3
BLOCK = 128


def butterfly_sum(value, axis, size, limit=None):
    stride = 1
    while stride < (limit or size):
        value = value + lax.ppermute(value, axis, [(i, i ^ stride) for i in range(size)])
        stride *= 2
    return value


def halving_steps(sizes):
    steps = []
    for axis, size in sizes:
        stride = size // 2
        while stride >= 1:
            steps.append((axis, size, stride))
            stride //= 2
    return steps


def halving_doubling_sum(value, sizes, middle=None, extra=()):
    steps = halving_steps(sizes) + list(extra)
    for axis, size, stride in steps:
        upper = (lax.axis_index(axis) // stride) % 2 == 1
        half = value.shape[0] // 2
        low, high = value[:half], value[half:]
        keep = jnp.where(upper, high, low)
        send = jnp.where(upper, low, high)
        value = keep + lax.ppermute(send, axis, [(i, i ^ stride) for i in range(size)])
    if middle is not None:
        value = middle(value)
    for axis, size, stride in reversed(steps):
        upper = (lax.axis_index(axis) // stride) % 2 == 1
        other = lax.ppermute(value, axis, [(i, i ^ stride) for i in range(size)])
        value = jnp.where(upper, jnp.concatenate([other, value]), jnp.concatenate([value, other]))
    return value


def body(species_field, initial):
    highest = lax.Precision.HIGHEST
    by_row = jnp.moveaxis(species_field, 2, 0)
    regrouped = lax.all_to_all(by_row, "gx", split_axis=0, concat_axis=0, tiled=True)
    x_blocks, species, block_x, slab_z = regrouped.shape
    rows_x = x_blocks * block_x
    fibers = jnp.swapaxes(regrouped, 0, 1).reshape(species, rows_x, slab_z)
    scale_one = 1.0 / (S * NY * NZ)
    n_blocks = rows_x // BLOCK
    lower = []
    for row in range(n_blocks):
        strip = jnp.einsum(
            "sxc,swc->xw",
            fibers[:, row * BLOCK:(row + 1) * BLOCK],
            fibers[:, :(row + 1) * BLOCK],
            precision=highest,
        ) * scale_one
        lower.extend(strip[:, col * BLOCK:(col + 1) * BLOCK] for col in range(row + 1))
    packed = jnp.concatenate(lower, axis=0)
    sizes = (("gx", lax.axis_size("gx")), ("gy", lax.axis_size("gy")))
    axis_y, size_y = sizes[1]
    packed = halving_doubling_sum(
        packed, sizes[:1], middle=lambda chunk: butterfly_sum(chunk, axis_y, size_y, size_y // 2),
        extra=((axis_y, size_y, size_y // 2),),
    )
    blocks = packed.reshape(-1, BLOCK, BLOCK)
    both = jnp.concatenate([blocks, jnp.swapaxes(blocks, 1, 2)], axis=0)
    index = {}
    for row in range(n_blocks):
        for col in range(row + 1):
            index[(row, col)] = len(index)
    picks = [[index[(row, col)] if col <= row else len(index) + index[(col, row)]
              for col in range(n_blocks)] for row in range(n_blocks)]
    tiles = jnp.take(both, jnp.asarray(picks, jnp.int32), axis=0)
    gram_one = jnp.swapaxes(tiles, 1, 2).reshape(rows_x, rows_x)
    basis = initial
    for sweep_index in range(SWEEPS):
        wide = jnp.dot(gram_one, basis, precision=highest, preferred_element_type=jnp.float32)
        square = jnp.dot(wide.T, wide, precision=highest, preferred_element_type=jnp.float32)
        factor_low = jnp.linalg.cholesky(square)
        basis = lax.linalg.triangular_solve(factor_low, wide, left_side=False, lower=True, transpose_a=True)
    core_tensor = jnp.einsum("xr,sxc->src", basis, fibers, precision=highest)
    n_gy = lax.axis_size("gy")
    n_gx = lax.axis_size("gx")
    pairs = core_tensor.reshape(n_gx * n_gy, -1, slab_z)
    gathered = lax.all_to_all(pairs, ("gx", "gy"), split_axis=0, concat_axis=0, tiled=True)
    columns = jnp.swapaxes(gathered.reshape(n_gx, n_gy, -1), 0, 1).reshape(n_gy * n_gx, -1)
    second_part = jnp.einsum("yc,wc->yw", columns, columns, precision=highest) / (S * R * NZ)
    half_y = second_part.shape[0] // 2
    lower_two = jnp.stack([second_part[:half_y, :half_y], second_part[half_y:, :half_y], second_part[half_y:, half_y:]])
    lower_two = butterfly_sum(lower_two, "gx", lax.axis_size("gx"))
    lower_two = butterfly_sum(lower_two, "gy", lax.axis_size("gy"))
    gram_two = jnp.concatenate([
        jnp.concatenate([lower_two[0], lower_two[1].T], axis=1),
        jnp.concatenate([lower_two[1], lower_two[2]], axis=1),
    ], axis=0)
    return (basis * math.sqrt(rows_x), gram_two)


def solution(mesh):
    placed = (P(None, "gx", "gy", None), P())
    return jax.shard_map(body, mesh=mesh, in_specs=placed, out_specs=(P(), P()), check_vma=False)
```
